256 devices in a mesh: row: 16 (over z, core), col: 16 (over x, y).
Axes of the slice: x: 4, y: 4, z: 8, core: 2. Of those that a mesh axis runs over, the one named last changes fastest.
Arguments:
- site_tensor: bfloat16 [1024, 4, 1024], P('row', None, 'col'), may hold values from -180 to 180
- site_tangent: bfloat16 [1024, 4, 1024], P('row', None, 'col'), may hold values from -180 to 180
- left_env: bfloat16 [1024, 16384], P('row', 'col'), may hold values from -0.1875 to 0.375
- right_env: bfloat16 [1024, 16384], P('row', 'col'), may hold values from -0.046875 to 0.09375
- mpo: bfloat16 [16, 16, 4, 4], replicated, may hold values from -0.25 to 0.75
- dissipation: float32 [4], replicated, may hold values from 0.2 to 2
Outputs:
- evolved: float32 [1024, 4, 1024], P('row', None, 'col')
- evolved_tangent: float32 [1024, 4, 1024], P('row', None, 'col')
The draws below stay inside these ranges and needn't reach their ends.
All inputs are finite; a program needn't handle non-finite values.
Results may differ from the reference program's by a relative error of at most 0.0055.
Values may be sent and summed in bfloat16 or wider, within the bound.
No kernel may reach another device: no remote copies, remote signals or barrier semaphores. Data moves between devices by JAX's collectives and lax.ppermute only.
A program may use at most 64 MiB of HBM per device.

```python
import math
import jax
import jax.numpy as jnp
from jax import lax

D = 1024
W = 16
PHYS = 4
KRYLOV = 3


def shaped_site(key):
    first, second, third = jax.random.split(key, 3)
    base = jax.random.truncated_normal(first, -6.0, 6.0, (D, PHYS, D), jnp.float32)
    ramp = 1.0 + 2.0 * jnp.arange(D, dtype=jnp.float32) / max(D - 1, 1)
    rowscale = jnp.exp(jax.random.uniform(second, (D,), jnp.float32, 0.0, math.log(10.0))) * ramp
    colscale = jnp.exp(jax.random.uniform(third, (D,), jnp.float32, 0.0, math.log(10.0)))
    return base * rowscale[:, None, None] * colscale[None, None, :] * 0.1


def draw_site_tensor(key, part):
    return shaped_site(jax.random.fold_in(key, 11)).astype(jnp.bfloat16)


def draw_site_tangent(key, part):
    return shaped_site(jax.random.fold_in(key, 23)).astype(jnp.bfloat16)


def environment(key, noise_scale, diagonal_value):
    noise = jax.random.truncated_normal(key, -6.0, 6.0, (D, D * W), jnp.float32)
    owner = jnp.arange(D * W, dtype=jnp.int32) // W
    onbond = (jnp.arange(D, dtype=jnp.int32)[:, None] == owner[None, :]).astype(jnp.float32)
    return noise * noise_scale + onbond * diagonal_value


def draw_left_env(key, part):
    return environment(jax.random.fold_in(key, 37), 1.0 / math.sqrt(D), 0.1875).astype(jnp.bfloat16)


def draw_right_env(key, part):
    return environment(jax.random.fold_in(key, 41), 1.0 / math.sqrt(W * D), 0.046875).astype(jnp.bfloat16)


def draw_mpo(key, part):
    inner_key = jax.random.fold_in(key, 53)
    noise = jax.random.truncated_normal(inner_key, -4.0, 4.0, (W, W, PHYS, PHYS), jnp.float32)
    return (0.25 + 0.125 * noise).astype(jnp.bfloat16)


def setup_inputs(seed: int = 0) -> dict:
    keys = jax.random.split(jax.random.key(seed), 7)
    return {
        "site_tensor": draw_site_tensor(jax.random.fold_in(keys[6], 71), 0),
        "site_tangent": draw_site_tangent(jax.random.fold_in(keys[6], 71), 0),
        "left_env": draw_left_env(jax.random.fold_in(keys[6], 71), 0),
        "right_env": draw_right_env(jax.random.fold_in(keys[6], 71), 0),
        "mpo": draw_mpo(jax.random.fold_in(keys[6], 71), 0),
        "dissipation": jnp.clip(jnp.exp(jax.random.uniform(keys[5], (PHYS,), jnp.float32, math.log(0.2), math.log(2.0))), 0.2, 2.0),
    }


taylor_order = 16

def apply_full(stacked, left_env, right_env, mpo, dissipation):
    size = stacked.shape[0]
    panels = stacked.shape[1]
    physical = stacked.shape[2]
    channels = mpo.shape[0]
    rounded = stacked.astype(jnp.bfloat16)
    flat = rounded.reshape(size, panels * physical * size)
    block = min(128, size)
    count = size // block
    left_blocks = left_env.reshape(count, block, size, channels)

    def one_block(left_block):
        mixed = lax.dot_general(left_block, flat, (((1,), (0,)), ((), ())), preferred_element_type=jnp.float32)
        mixed = mixed.astype(jnp.bfloat16).reshape(block, channels, panels, physical, size)
        channel = jnp.einsum('awspr,wvpq->asqrv', mixed.astype(jnp.float32), mpo.astype(jnp.float32))
        channel = channel.astype(jnp.bfloat16).reshape(block * panels * physical, size * channels)
        return lax.dot_general(channel, right_env, (((1,), (1,)), ((), ())), preferred_element_type=jnp.float32)
    result = lax.map(one_block, left_blocks).reshape(size, panels, physical, size)
    return result - dissipation[None, None, :, None] * stacked

def taylor(hess, dhess):
    size = hess.shape[0]
    term = jnp.zeros((size,), jnp.float32).at[0].set(1.0)
    dterm = jnp.zeros((size,), jnp.float32)
    total = term
    dtotal = dterm
    for order in range(1, taylor_order + 1):
        nterm = jnp.dot(hess, term, precision=lax.Precision.HIGHEST) / order
        dterm = (jnp.dot(dhess, term, precision=lax.Precision.HIGHEST) + jnp.dot(hess, dterm, precision=lax.Precision.HIGHEST)) / order
        term = nterm
        total = total + term
        dtotal = dtotal + dterm
    return (total, dtotal)

def reference(site_tensor, site_tangent, left_env, right_env, mpo, dissipation):
    primal = site_tensor.astype(jnp.float32)
    tangent = site_tangent.astype(jnp.float32)
    norm_site = jnp.sqrt(jnp.sum(primal * primal))
    norm_tangent = jnp.sum(primal * tangent) / norm_site
    basis = [primal / norm_site]
    tangents = [(tangent - basis[0] * norm_tangent) / norm_site]
    hess = jnp.zeros((KRYLOV, KRYLOV), jnp.float32)
    dhess = jnp.zeros((KRYLOV, KRYLOV), jnp.float32)
    for level in range(KRYLOV):
        both = apply_full(jnp.stack([basis[level], tangents[level]], axis=1), left_env, right_env, mpo, dissipation)
        image = both[:, 0]
        dimage = both[:, 1]
        coeffs = jnp.stack([jnp.sum(vector * image) for vector in basis])
        dcoeffs = jnp.stack([jnp.sum(tangents[index] * image) + jnp.sum(basis[index] * dimage) for index in range(level + 1)])
        hess = hess.at[:level + 1, level].set(coeffs)
        dhess = dhess.at[:level + 1, level].set(dcoeffs)
        if level + 1 < KRYLOV:
            residual = image
            dresidual = dimage
            for index in range(level + 1):
                residual = residual - coeffs[index] * basis[index]
                dresidual = dresidual - dcoeffs[index] * basis[index] - coeffs[index] * tangents[index]
            height = jnp.sqrt(jnp.sum(residual * residual))
            dheight = jnp.sum(residual * dresidual) / height
            newvec = residual / height
            basis.append(newvec)
            tangents.append((dresidual - newvec * dheight) / height)
            hess = hess.at[level + 1, level].set(height)
            dhess = dhess.at[level + 1, level].set(dheight)
    coeff, dcoeff = taylor(hess, dhess)
    spread = jnp.zeros_like(primal)
    dspread = jnp.zeros_like(primal)
    for index in range(KRYLOV):
        spread = spread + coeff[index] * basis[index]
        dspread = dspread + coeff[index] * tangents[index] + dcoeff[index] * basis[index]
    evolved = norm_site * spread
    evolved_tangent = norm_tangent * spread + norm_site * dspread
    return (evolved, evolved_tangent)
```

```python
import jax
import jax.numpy as jnp
from jax import lax
from jax.sharding import PartitionSpec as P

KRYLOV = 3


taylor_order = 16


def inner(first, second):
    return jnp.sum(first * second)


def total(values):
    return lax.psum(lax.psum(values, "col"), "row")


def taylor(hess, dhess):
    size = hess.shape[0]
    term = jnp.zeros((size,), jnp.float32).at[0].set(1.0)
    dterm = jnp.zeros((size,), jnp.float32)
    total = term
    dtotal = dterm
    for order in range(1, taylor_order + 1):
        nterm = jnp.dot(hess, term, precision=lax.Precision.HIGHEST) / order
        dterm = (
            jnp.dot(dhess, term, precision=lax.Precision.HIGHEST)
            + jnp.dot(hess, dterm, precision=lax.Precision.HIGHEST)
        ) / order
        term = nterm
        total = total + term
        dtotal = dtotal + dterm
    return (total, dtotal)


def local(site_tensor, site_tangent, left_env, right_env, mpo, dissipation):
    rows_here, physical, cols_here = site_tensor.shape
    channels = mpo.shape[0]
    left_whole = lax.all_gather(left_env, "col", axis=1, tiled=True)
    right_whole = lax.all_gather(right_env, "row", axis=0, tiled=True)

    def apply(stacked):
        panels = stacked.shape[1]
        whole = lax.all_gather(stacked.astype(jnp.bfloat16), "row", axis=0, tiled=True)
        flat = whole.reshape(whole.shape[0], panels * physical * cols_here)
        left_three = left_whole.reshape(rows_here, flat.shape[0], channels)
        mixed = lax.dot_general(
            left_three, flat, (((1,), (0,)), ((), ())), preferred_element_type=jnp.float32
        )
        mixed = mixed.astype(jnp.bfloat16).reshape(rows_here, channels, panels, physical, cols_here)
        channel = jnp.einsum("awspr,wvpq->asqrv", mixed, mpo, preferred_element_type=jnp.float32)
        channel = channel.astype(jnp.bfloat16).reshape(
            rows_here * panels * physical, cols_here * channels
        )
        partial_rows = lax.dot_general(
            channel, right_whole, (((1,), (1,)), ((), ())), preferred_element_type=jnp.float32
        )
        partial_rows = partial_rows.reshape(rows_here, panels, physical, partial_rows.shape[1])
        summed = lax.psum_scatter(partial_rows, "col", scatter_dimension=3, tiled=True)
        return summed - dissipation[None, None, :, None] * stacked

    primal = site_tensor.astype(jnp.float32)
    tangent = site_tangent.astype(jnp.float32)
    starting = total(jnp.stack([inner(primal, primal), inner(primal, tangent)]))
    norm_site = jnp.sqrt(starting[0])
    norm_tangent = starting[1] / norm_site
    basis = [primal / norm_site]
    tangents = [(tangent - basis[0] * norm_tangent) / norm_site]
    hess = jnp.zeros((KRYLOV, KRYLOV), jnp.float32)
    dhess = jnp.zeros((KRYLOV, KRYLOV), jnp.float32)
    gram = jnp.zeros((KRYLOV, KRYLOV), jnp.float32)
    cross = jnp.zeros((KRYLOV, KRYLOV), jnp.float32)
    for level in range(KRYLOV):
        both = apply(jnp.stack([basis[level], tangents[level]], axis=1))
        image = both[:, 0]
        dimage = both[:, 1]
        counted = level + 1
        locals_list = [inner(vector, image) for vector in basis]
        locals_list = locals_list + [inner(vector, image) for vector in tangents]
        locals_list = locals_list + [inner(vector, dimage) for vector in basis]
        last = level + 1 == KRYLOV
        if not last:
            newest = basis[level]
            locals_list = locals_list + [inner(image, image), inner(image, dimage)]
            locals_list = locals_list + [inner(newest, vector) for vector in basis]
            locals_list = locals_list + [inner(newest, vector) for vector in tangents]
            locals_list = locals_list + [inner(vector, tangents[level]) for vector in basis[:level]]
        totals = total(jnp.stack(locals_list))
        coeffs = totals[:counted]
        across = totals[counted : 2 * counted]
        along = totals[2 * counted : 3 * counted]
        dcoeffs = across + along
        hess = hess.at[:counted, level].set(coeffs)
        dhess = dhess.at[:counted, level].set(dcoeffs)
        if not last:
            at = 3 * counted
            squared_image = totals[at]
            image_dimage = totals[at + 1]
            at += 2
            gram = gram.at[level, :counted].set(totals[at : at + counted])
            gram = gram.at[:counted, level].set(totals[at : at + counted])
            at += counted
            cross = cross.at[level, :counted].set(totals[at : at + counted])
            at += counted
            cross = cross.at[:level, level].set(totals[at : at + level])
            g = gram[:counted, :counted]
            t = cross[:counted, :counted]
            squared = (
                squared_image
                - 2.0 * jnp.sum(coeffs * coeffs)
                + jnp.dot(coeffs, jnp.dot(g, coeffs, precision=lax.Precision.HIGHEST), precision=lax.Precision.HIGHEST)
            )
            mixed_term = (
                image_dimage
                - jnp.sum(dcoeffs * coeffs)
                - jnp.sum(coeffs * across)
                - jnp.sum(coeffs * along)
                + jnp.dot(coeffs, jnp.dot(g, dcoeffs, precision=lax.Precision.HIGHEST), precision=lax.Precision.HIGHEST)
                + jnp.dot(coeffs, jnp.dot(t, coeffs, precision=lax.Precision.HIGHEST), precision=lax.Precision.HIGHEST)
            )
            residual = image
            dresidual = dimage
            for index in range(counted):
                residual = residual - coeffs[index] * basis[index]
                dresidual = (
                    dresidual - dcoeffs[index] * basis[index] - coeffs[index] * tangents[index]
                )
            height = jnp.sqrt(squared)
            dheight = mixed_term / height
            newvec = residual / height
            basis.append(newvec)
            tangents.append((dresidual - newvec * dheight) / height)
            hess = hess.at[level + 1, level].set(height)
            dhess = dhess.at[level + 1, level].set(dheight)
    coeff, dcoeff = taylor(hess, dhess)
    spread = jnp.zeros_like(primal)
    dspread = jnp.zeros_like(primal)
    for index in range(KRYLOV):
        spread = spread + coeff[index] * basis[index]
        dspread = dspread + coeff[index] * tangents[index] + dcoeff[index] * basis[index]
    evolved = norm_site * spread
    evolved_tangent = norm_tangent * spread + norm_site * dspread
    return (evolved, evolved_tangent)


def solution(mesh):
    in_specs = (
        P("row", None, "col"),
        P("row", None, "col"),
        P("row", "col"),
        P("row", "col"),
        P(),
        P(),
    )
    out_specs = (P("row", None, "col"), P("row", None, "col"))
    return jax.shard_map(local, mesh=mesh, in_specs=in_specs, out_specs=out_specs, check_vma=False)
```

```python
import jax
import jax.numpy as jnp
from jax import lax
from jax.sharding import PartitionSpec as P

KRYLOV = 3


taylor_order = 16


def inner(first, second):
    return jnp.sum(first * second)


def total(values):
    return lax.psum(lax.psum(values, "col"), "row")


def taylor(hess, dhess):
    size = hess.shape[0]
    term = jnp.zeros((size,), jnp.float32).at[0].set(1.0)
    dterm = jnp.zeros((size,), jnp.float32)
    total = term
    dtotal = dterm
    for order in range(1, taylor_order + 1):
        nterm = jnp.dot(hess, term, precision=lax.Precision.HIGHEST) / order
        dterm = (
            jnp.dot(dhess, term, precision=lax.Precision.HIGHEST)
            + jnp.dot(hess, dterm, precision=lax.Precision.HIGHEST)
        ) / order
        term = nterm
        total = total + term
        dtotal = dtotal + dterm
    return (total, dtotal)


def local(site_tensor, site_tangent, left_env, right_env, mpo, dissipation):
    rows_here, physical, cols_here = site_tensor.shape
    channels = mpo.shape[0]
    left_whole = lax.all_gather(left_env, "col", axis=1, tiled=True)
    right_whole = lax.all_gather(right_env, "row", axis=0, tiled=True)

    def apply(stacked):
        panels = stacked.shape[1]
        whole = lax.all_gather(stacked.astype(jnp.bfloat16), "row", axis=0, tiled=True)
        flat = whole.reshape(whole.shape[0], panels * physical * cols_here)
        left_three = left_whole.reshape(rows_here, flat.shape[0], channels)
        mixed = lax.dot_general(
            left_three, flat, (((1,), (0,)), ((), ())), preferred_element_type=jnp.float32
        )
        mixed = mixed.astype(jnp.bfloat16).reshape(rows_here, channels, panels, physical, cols_here)
        channel = jnp.einsum("awspr,wvpq->asqrv", mixed, mpo, preferred_element_type=jnp.float32)
        channel = channel.astype(jnp.bfloat16).reshape(
            rows_here * panels * physical, cols_here * channels
        )
        partial_rows = lax.dot_general(
            channel, right_whole, (((1,), (1,)), ((), ())), preferred_element_type=jnp.float32
        )
        partial_rows = partial_rows.reshape(rows_here, panels, physical, partial_rows.shape[1])
        blocks = lax.psum(1, "col")
        split = partial_rows.reshape(
            rows_here, panels, physical, blocks, partial_rows.shape[3] // blocks
        )
        summed = jnp.sum(lax.all_to_all(split, "col", 3, 3, tiled=False), axis=3)
        return summed - dissipation[None, None, :, None] * stacked

    primal = site_tensor.astype(jnp.float32)
    tangent = site_tangent.astype(jnp.float32)
    starting = total(jnp.stack([inner(primal, primal), inner(primal, tangent)]))
    norm_site = jnp.sqrt(starting[0])
    norm_tangent = starting[1] / norm_site
    basis = [primal / norm_site]
    tangents = [(tangent - basis[0] * norm_tangent) / norm_site]
    hess = jnp.zeros((KRYLOV, KRYLOV), jnp.float32)
    dhess = jnp.zeros((KRYLOV, KRYLOV), jnp.float32)
    gram = jnp.zeros((KRYLOV, KRYLOV), jnp.float32)
    cross = jnp.zeros((KRYLOV, KRYLOV), jnp.float32)
    for level in range(KRYLOV):
        both = apply(jnp.stack([basis[level], tangents[level]], axis=1))
        image = both[:, 0]
        dimage = both[:, 1]
        counted = level + 1
        locals_list = [inner(vector, image) for vector in basis]
        locals_list = locals_list + [inner(vector, image) for vector in tangents]
        locals_list = locals_list + [inner(vector, dimage) for vector in basis]
        last = level + 1 == KRYLOV
        if not last:
            newest = basis[level]
            locals_list = locals_list + [inner(image, image), inner(image, dimage)]
            locals_list = locals_list + [inner(newest, vector) for vector in basis]
            locals_list = locals_list + [inner(newest, vector) for vector in tangents]
            locals_list = locals_list + [inner(vector, tangents[level]) for vector in basis[:level]]
        totals = total(jnp.stack(locals_list))
        coeffs = totals[:counted]
        across = totals[counted : 2 * counted]
        along = totals[2 * counted : 3 * counted]
        dcoeffs = across + along
        hess = hess.at[:counted, level].set(coeffs)
        dhess = dhess.at[:counted, level].set(dcoeffs)
        if not last:
            at = 3 * counted
            squared_image = totals[at]
            image_dimage = totals[at + 1]
            at += 2
            gram = gram.at[level, :counted].set(totals[at : at + counted])
            gram = gram.at[:counted, level].set(totals[at : at + counted])
            at += counted
            cross = cross.at[level, :counted].set(totals[at : at + counted])
            at += counted
            cross = cross.at[:level, level].set(totals[at : at + level])
            g = gram[:counted, :counted]
            t = cross[:counted, :counted]
            squared = (
                squared_image
                - 2.0 * jnp.sum(coeffs * coeffs)
                + jnp.dot(coeffs, jnp.dot(g, coeffs, precision=lax.Precision.HIGHEST), precision=lax.Precision.HIGHEST)
            )
            mixed_term = (
                image_dimage
                - jnp.sum(dcoeffs * coeffs)
                - jnp.sum(coeffs * across)
                - jnp.sum(coeffs * along)
                + jnp.dot(coeffs, jnp.dot(g, dcoeffs, precision=lax.Precision.HIGHEST), precision=lax.Precision.HIGHEST)
                + jnp.dot(coeffs, jnp.dot(t, coeffs, precision=lax.Precision.HIGHEST), precision=lax.Precision.HIGHEST)
            )
            residual = image
            dresidual = dimage
            for index in range(counted):
                residual = residual - coeffs[index] * basis[index]
                dresidual = (
                    dresidual - dcoeffs[index] * basis[index] - coeffs[index] * tangents[index]
                )
            height = jnp.sqrt(squared)
            dheight = mixed_term / height
            newvec = residual / height
            basis.append(newvec)
            tangents.append((dresidual - newvec * dheight) / height)
            hess = hess.at[level + 1, level].set(height)
            dhess = dhess.at[level + 1, level].set(dheight)
    coeff, dcoeff = taylor(hess, dhess)
    spread = jnp.zeros_like(primal)
    dspread = jnp.zeros_like(primal)
    for index in range(KRYLOV):
        spread = spread + coeff[index] * basis[index]
        dspread = dspread + coeff[index] * tangents[index] + dcoeff[index] * basis[index]
    evolved = norm_site * spread
    evolved_tangent = norm_tangent * spread + norm_site * dspread
    return (evolved, evolved_tangent)


def solution(mesh):
    in_specs = (
        P("row", None, "col"),
        P("row", None, "col"),
        P("row", "col"),
        P("row", "col"),
        P(),
        P(),
    )
    out_specs = (P("row", None, "col"), P("row", None, "col"))
    return jax.shard_map(local, mesh=mesh, in_specs=in_specs, out_specs=out_specs, check_vma=False)
```

```python
import jax
import jax.numpy as jnp
from jax import lax
from jax.sharding import PartitionSpec as P

KRYLOV = 3


taylor_order = 16


def inner(first, second):
    return jnp.sum(first * second)


def total(values):
    return lax.psum(lax.psum(values, "col"), "row")


def taylor(hess, dhess):
    size = hess.shape[0]
    term = jnp.zeros((size,), jnp.float32).at[0].set(1.0)
    dterm = jnp.zeros((size,), jnp.float32)
    total = term
    dtotal = dterm
    for order in range(1, taylor_order + 1):
        nterm = jnp.dot(hess, term, precision=lax.Precision.HIGHEST) / order
        dterm = (
            jnp.dot(dhess, term, precision=lax.Precision.HIGHEST)
            + jnp.dot(hess, dterm, precision=lax.Precision.HIGHEST)
        ) / order
        term = nterm
        total = total + term
        dtotal = dtotal + dterm
    return (total, dtotal)


def local(site_tensor, site_tangent, left_env, right_env, mpo, dissipation):
    rows_here, physical, cols_here = site_tensor.shape
    channels = mpo.shape[0]
    left_whole = lax.all_gather(left_env, "col", axis=1, tiled=True)
    right_whole = lax.all_gather(right_env, "row", axis=0, tiled=True)

    def apply(stacked, whole_stacked):
        panels = stacked.shape[1]
        whole = whole_stacked.astype(jnp.bfloat16)
        flat = whole.reshape(whole.shape[0], panels * physical * cols_here)
        left_three = left_whole.reshape(rows_here, flat.shape[0], channels)
        mixed = lax.dot_general(
            left_three, flat, (((1,), (0,)), ((), ())), preferred_element_type=jnp.float32
        )
        mixed = mixed.astype(jnp.bfloat16).reshape(rows_here, channels, panels, physical, cols_here)
        channel = jnp.einsum("awspr,wvpq->asqrv", mixed, mpo, preferred_element_type=jnp.float32)
        channel = channel.astype(jnp.bfloat16).reshape(
            rows_here * panels * physical, cols_here * channels
        )
        partial_rows = lax.dot_general(
            channel, right_whole, (((1,), (1,)), ((), ())), preferred_element_type=jnp.float32
        )
        partial_rows = partial_rows.reshape(rows_here, panels, physical, partial_rows.shape[1])
        blocks = lax.psum(1, "col")
        split = partial_rows.reshape(
            rows_here, panels, physical, blocks, partial_rows.shape[3] // blocks
        )
        summed = jnp.sum(lax.all_to_all(split, "col", 3, 3, tiled=False), axis=3)
        return summed - dissipation[None, None, :, None] * stacked

    primal = site_tensor.astype(jnp.float32)
    tangent = site_tangent.astype(jnp.float32)
    starting = total(jnp.stack([inner(primal, primal), inner(primal, tangent)]))
    norm_site = jnp.sqrt(starting[0])
    norm_tangent = starting[1] / norm_site
    basis = [primal / norm_site]
    tangents = [(tangent - basis[0] * norm_tangent) / norm_site]
    inputs_whole = lax.all_gather(
        jnp.stack([site_tensor, site_tangent], axis=1), "row", axis=0, tiled=True
    ).astype(jnp.float32)
    primal_whole = inputs_whole[:, 0]
    tangent_whole = inputs_whole[:, 1]
    basis_whole = [primal_whole / norm_site]
    tangents_whole = [(tangent_whole - basis_whole[0] * norm_tangent) / norm_site]
    hess = jnp.zeros((KRYLOV, KRYLOV), jnp.float32)
    dhess = jnp.zeros((KRYLOV, KRYLOV), jnp.float32)
    gram = jnp.zeros((KRYLOV, KRYLOV), jnp.float32)
    cross = jnp.zeros((KRYLOV, KRYLOV), jnp.float32)
    for level in range(KRYLOV):
        both = apply(
            jnp.stack([basis[level], tangents[level]], axis=1),
            jnp.stack([basis_whole[level], tangents_whole[level]], axis=1),
        )
        image = both[:, 0]
        dimage = both[:, 1]
        if level + 1 < KRYLOV:
            both_whole = lax.all_gather(both, "row", axis=0, tiled=True)
            image_whole = both_whole[:, 0]
            dimage_whole = both_whole[:, 1]
        counted = level + 1
        locals_list = [inner(vector, image) for vector in basis]
        locals_list = locals_list + [inner(vector, image) for vector in tangents]
        locals_list = locals_list + [inner(vector, dimage) for vector in basis]
        last = level + 1 == KRYLOV
        if not last:
            newest = basis[level]
            locals_list = locals_list + [inner(image, image), inner(image, dimage)]
            locals_list = locals_list + [inner(newest, vector) for vector in basis]
            locals_list = locals_list + [inner(newest, vector) for vector in tangents]
            locals_list = locals_list + [inner(vector, tangents[level]) for vector in basis[:level]]
        totals = total(jnp.stack(locals_list))
        coeffs = totals[:counted]
        across = totals[counted : 2 * counted]
        along = totals[2 * counted : 3 * counted]
        dcoeffs = across + along
        hess = hess.at[:counted, level].set(coeffs)
        dhess = dhess.at[:counted, level].set(dcoeffs)
        if not last:
            at = 3 * counted
            squared_image = totals[at]
            image_dimage = totals[at + 1]
            at += 2
            gram = gram.at[level, :counted].set(totals[at : at + counted])
            gram = gram.at[:counted, level].set(totals[at : at + counted])
            at += counted
            cross = cross.at[level, :counted].set(totals[at : at + counted])
            at += counted
            cross = cross.at[:level, level].set(totals[at : at + level])
            g = gram[:counted, :counted]
            t = cross[:counted, :counted]
            squared = (
                squared_image
                - 2.0 * jnp.sum(coeffs * coeffs)
                + jnp.dot(coeffs, jnp.dot(g, coeffs, precision=lax.Precision.HIGHEST), precision=lax.Precision.HIGHEST)
            )
            mixed_term = (
                image_dimage
                - jnp.sum(dcoeffs * coeffs)
                - jnp.sum(coeffs * across)
                - jnp.sum(coeffs * along)
                + jnp.dot(coeffs, jnp.dot(g, dcoeffs, precision=lax.Precision.HIGHEST), precision=lax.Precision.HIGHEST)
                + jnp.dot(coeffs, jnp.dot(t, coeffs, precision=lax.Precision.HIGHEST), precision=lax.Precision.HIGHEST)
            )
            residual = image
            dresidual = dimage
            for index in range(counted):
                residual = residual - coeffs[index] * basis[index]
                dresidual = (
                    dresidual - dcoeffs[index] * basis[index] - coeffs[index] * tangents[index]
                )
            height = jnp.sqrt(squared)
            dheight = mixed_term / height
            newvec = residual / height
            basis.append(newvec)
            tangents.append((dresidual - newvec * dheight) / height)
            residual_whole = image_whole
            dresidual_whole = dimage_whole
            for index in range(counted):
                residual_whole = residual_whole - coeffs[index] * basis_whole[index]
                dresidual_whole = (
                    dresidual_whole
                    - dcoeffs[index] * basis_whole[index]
                    - coeffs[index] * tangents_whole[index]
                )
            newvec_whole = residual_whole / height
            basis_whole.append(newvec_whole)
            tangents_whole.append((dresidual_whole - newvec_whole * dheight) / height)
            hess = hess.at[level + 1, level].set(height)
            dhess = dhess.at[level + 1, level].set(dheight)
    coeff, dcoeff = taylor(hess, dhess)
    spread = jnp.zeros_like(primal)
    dspread = jnp.zeros_like(primal)
    for index in range(KRYLOV):
        spread = spread + coeff[index] * basis[index]
        dspread = dspread + coeff[index] * tangents[index] + dcoeff[index] * basis[index]
    evolved = norm_site * spread
    evolved_tangent = norm_tangent * spread + norm_site * dspread
    return (evolved, evolved_tangent)


def solution(mesh):
    in_specs = (
        P("row", None, "col"),
        P("row", None, "col"),
        P("row", "col"),
        P("row", "col"),
        P(),
        P(),
    )
    out_specs = (P("row", None, "col"), P("row", None, "col"))
    return jax.shard_map(local, mesh=mesh, in_specs=in_specs, out_specs=out_specs, check_vma=False)
```

```python
import jax
import jax.numpy as jnp
from jax import lax
from jax.sharding import PartitionSpec as P

KRYLOV = 3


taylor_order = 16


def inner(first, second):
    return jnp.sum(first * second)


def total(values):
    return lax.psum(lax.psum(values, "col"), "row")


def taylor(hess, dhess):
    size = hess.shape[0]
    term = jnp.zeros((size,), jnp.float32).at[0].set(1.0)
    dterm = jnp.zeros((size,), jnp.float32)
    total = term
    dtotal = dterm
    for order in range(1, taylor_order + 1):
        nterm = jnp.dot(hess, term, precision=lax.Precision.HIGHEST) / order
        dterm = (
            jnp.dot(dhess, term, precision=lax.Precision.HIGHEST)
            + jnp.dot(hess, dterm, precision=lax.Precision.HIGHEST)
        ) / order
        term = nterm
        total = total + term
        dtotal = dtotal + dterm
    return (total, dtotal)


def local(site_tensor, site_tangent, left_env, right_env, mpo, dissipation):
    rows_here, physical, cols_here = site_tensor.shape
    channels = mpo.shape[0]
    left_whole = lax.all_gather(left_env, "col", axis=1, tiled=True)
    right_whole = lax.all_gather(right_env, "row", axis=0, tiled=True)

    def apply(stacked, whole_stacked):
        panels = stacked.shape[1]
        whole = whole_stacked.astype(jnp.bfloat16)
        flat = whole.reshape(whole.shape[0], panels * physical * cols_here)
        left_three = left_whole.reshape(rows_here, flat.shape[0], channels)
        mixed = lax.dot_general(
            left_three, flat, (((1,), (0,)), ((), ())), preferred_element_type=jnp.float32
        )
        mixed = mixed.astype(jnp.bfloat16).reshape(rows_here, channels, panels, physical, cols_here)
        channel = jnp.einsum("awspr,wvpq->asqrv", mixed, mpo, preferred_element_type=jnp.float32)
        channel = channel.astype(jnp.bfloat16).reshape(
            rows_here * panels * physical, cols_here * channels
        )
        partial_cols = lax.dot_general(
            right_whole, channel, (((1,), (1,)), ((), ())), preferred_element_type=jnp.float32
        )
        blocks = lax.psum(1, "col")
        split = partial_cols.reshape(blocks, partial_cols.shape[0] // blocks, channel.shape[0])
        gathered = lax.all_to_all(split, "col", 0, 0, tiled=False)
        summed = jnp.sum(gathered, axis=0).reshape(cols_here, rows_here, panels, physical)
        summed = jnp.transpose(summed, (1, 2, 3, 0))
        return summed - dissipation[None, None, :, None] * stacked

    primal = site_tensor.astype(jnp.float32)
    tangent = site_tangent.astype(jnp.float32)
    starting = total(jnp.stack([inner(primal, primal), inner(primal, tangent)]))
    norm_site = jnp.sqrt(starting[0])
    norm_tangent = starting[1] / norm_site
    basis = [primal / norm_site]
    tangents = [(tangent - basis[0] * norm_tangent) / norm_site]
    inputs_whole = lax.all_gather(
        jnp.stack([site_tensor, site_tangent], axis=1), "row", axis=0, tiled=True
    ).astype(jnp.float32)
    primal_whole = inputs_whole[:, 0]
    tangent_whole = inputs_whole[:, 1]
    basis_whole = [primal_whole / norm_site]
    tangents_whole = [(tangent_whole - basis_whole[0] * norm_tangent) / norm_site]
    hess = jnp.zeros((KRYLOV, KRYLOV), jnp.float32)
    dhess = jnp.zeros((KRYLOV, KRYLOV), jnp.float32)
    gram = jnp.zeros((KRYLOV, KRYLOV), jnp.float32)
    cross = jnp.zeros((KRYLOV, KRYLOV), jnp.float32)
    for level in range(KRYLOV):
        both = apply(
            jnp.stack([basis[level], tangents[level]], axis=1),
            jnp.stack([basis_whole[level], tangents_whole[level]], axis=1),
        )
        image = both[:, 0]
        dimage = both[:, 1]
        if level + 1 < KRYLOV:
            both_whole = lax.all_gather(both, "row", axis=0, tiled=True)
            image_whole = both_whole[:, 0]
            dimage_whole = both_whole[:, 1]
        counted = level + 1
        locals_list = [inner(vector, image) for vector in basis]
        locals_list = locals_list + [inner(vector, image) for vector in tangents]
        locals_list = locals_list + [inner(vector, dimage) for vector in basis]
        last = level + 1 == KRYLOV
        if not last:
            newest = basis[level]
            locals_list = locals_list + [inner(image, image), inner(image, dimage)]
            locals_list = locals_list + [inner(newest, vector) for vector in basis]
            locals_list = locals_list + [inner(newest, vector) for vector in tangents]
            locals_list = locals_list + [inner(vector, tangents[level]) for vector in basis[:level]]
        totals = total(jnp.stack(locals_list))
        coeffs = totals[:counted]
        across = totals[counted : 2 * counted]
        along = totals[2 * counted : 3 * counted]
        dcoeffs = across + along
        hess = hess.at[:counted, level].set(coeffs)
        dhess = dhess.at[:counted, level].set(dcoeffs)
        if not last:
            at = 3 * counted
            squared_image = totals[at]
            image_dimage = totals[at + 1]
            at += 2
            gram = gram.at[level, :counted].set(totals[at : at + counted])
            gram = gram.at[:counted, level].set(totals[at : at + counted])
            at += counted
            cross = cross.at[level, :counted].set(totals[at : at + counted])
            at += counted
            cross = cross.at[:level, level].set(totals[at : at + level])
            g = gram[:counted, :counted]
            t = cross[:counted, :counted]
            squared = (
                squared_image
                - 2.0 * jnp.sum(coeffs * coeffs)
                + jnp.dot(coeffs, jnp.dot(g, coeffs, precision=lax.Precision.HIGHEST), precision=lax.Precision.HIGHEST)
            )
            mixed_term = (
                image_dimage
                - jnp.sum(dcoeffs * coeffs)
                - jnp.sum(coeffs * across)
                - jnp.sum(coeffs * along)
                + jnp.dot(coeffs, jnp.dot(g, dcoeffs, precision=lax.Precision.HIGHEST), precision=lax.Precision.HIGHEST)
                + jnp.dot(coeffs, jnp.dot(t, coeffs, precision=lax.Precision.HIGHEST), precision=lax.Precision.HIGHEST)
            )
            residual = image
            dresidual = dimage
            for index in range(counted):
                residual = residual - coeffs[index] * basis[index]
                dresidual = (
                    dresidual - dcoeffs[index] * basis[index] - coeffs[index] * tangents[index]
                )
            height = jnp.sqrt(squared)
            dheight = mixed_term / height
            newvec = residual / height
            basis.append(newvec)
            tangents.append((dresidual - newvec * dheight) / height)
            residual_whole = image_whole
            dresidual_whole = dimage_whole
            for index in range(counted):
                residual_whole = residual_whole - coeffs[index] * basis_whole[index]
                dresidual_whole = (
                    dresidual_whole
                    - dcoeffs[index] * basis_whole[index]
                    - coeffs[index] * tangents_whole[index]
                )
            newvec_whole = residual_whole / height
            basis_whole.append(newvec_whole)
            tangents_whole.append((dresidual_whole - newvec_whole * dheight) / height)
            hess = hess.at[level + 1, level].set(height)
            dhess = dhess.at[level + 1, level].set(dheight)
    coeff, dcoeff = taylor(hess, dhess)
    spread = jnp.zeros_like(primal)
    dspread = jnp.zeros_like(primal)
    for index in range(KRYLOV):
        spread = spread + coeff[index] * basis[index]
        dspread = dspread + coeff[index] * tangents[index] + dcoeff[index] * basis[index]
    evolved = norm_site * spread
    evolved_tangent = norm_tangent * spread + norm_site * dspread
    return (evolved, evolved_tangent)


def solution(mesh):
    in_specs = (
        P("row", None, "col"),
        P("row", None, "col"),
        P("row", "col"),
        P("row", "col"),
        P(),
        P(),
    )
    out_specs = (P("row", None, "col"), P("row", None, "col"))
    return jax.shard_map(local, mesh=mesh, in_specs=in_specs, out_specs=out_specs, check_vma=False)
```

```python
import jax
import jax.numpy as jnp
from jax import lax
from jax.sharding import PartitionSpec as P

KRYLOV = 3


taylor_order = 16


def inner(first, second):
    return jnp.sum(first * second)


def total(values):
    return lax.psum(lax.psum(values, "col"), "row")


def taylor(hess, dhess):
    size = hess.shape[0]
    term = jnp.zeros((size,), jnp.float32).at[0].set(1.0)
    dterm = jnp.zeros((size,), jnp.float32)
    total = term
    dtotal = dterm
    for order in range(1, taylor_order + 1):
        nterm = jnp.dot(hess, term, precision=lax.Precision.HIGHEST) / order
        dterm = (
            jnp.dot(dhess, term, precision=lax.Precision.HIGHEST)
            + jnp.dot(hess, dterm, precision=lax.Precision.HIGHEST)
        ) / order
        term = nterm
        total = total + term
        dtotal = dtotal + dterm
    return (total, dtotal)


def local(site_tensor, site_tangent, left_env, right_env, mpo, dissipation):
    rows_here, physical, cols_here = site_tensor.shape
    channels = mpo.shape[0]
    left_whole = lax.all_gather(left_env, "col", axis=1, tiled=True)
    right_whole = lax.all_gather(right_env, "row", axis=0, tiled=True)
    right_whole = jnp.transpose(
        right_whole.reshape(right_whole.shape[0], cols_here, channels), (0, 2, 1)
    ).reshape(right_whole.shape[0], channels * cols_here)

    def apply(stacked, whole_stacked):
        panels = stacked.shape[1]
        whole = whole_stacked.astype(jnp.bfloat16)
        flat = whole.reshape(whole.shape[0], panels * physical * cols_here)
        left_three = left_whole.reshape(rows_here, flat.shape[0], channels)
        mixed = lax.dot_general(
            left_three, flat, (((1,), (0,)), ((), ())), preferred_element_type=jnp.float32
        )
        mixed = mixed.astype(jnp.bfloat16).reshape(rows_here, channels, panels, physical, cols_here)
        channel = jnp.einsum("awspr,wvpq->asqvr", mixed, mpo, preferred_element_type=jnp.float32)
        channel = channel.astype(jnp.bfloat16).reshape(
            rows_here * panels * physical, cols_here * channels
        )
        partial_cols = lax.dot_general(
            right_whole, channel, (((1,), (1,)), ((), ())), preferred_element_type=jnp.float32
        )
        blocks = lax.psum(1, "col")
        split = partial_cols.reshape(blocks, partial_cols.shape[0] // blocks, channel.shape[0])
        gathered = lax.all_to_all(split, "col", 0, 0, tiled=False)
        summed = jnp.sum(gathered, axis=0).reshape(cols_here, rows_here, panels, physical)
        summed = jnp.transpose(summed, (1, 2, 3, 0))
        return summed - dissipation[None, None, :, None] * stacked

    primal = site_tensor.astype(jnp.float32)
    tangent = site_tangent.astype(jnp.float32)
    starting = total(jnp.stack([inner(primal, primal), inner(primal, tangent)]))
    norm_site = jnp.sqrt(starting[0])
    norm_tangent = starting[1] / norm_site
    basis = [primal / norm_site]
    tangents = [(tangent - basis[0] * norm_tangent) / norm_site]
    inputs_whole = lax.all_gather(
        jnp.stack([site_tensor, site_tangent], axis=1), "row", axis=0, tiled=True
    ).astype(jnp.float32)
    primal_whole = inputs_whole[:, 0]
    tangent_whole = inputs_whole[:, 1]
    basis_whole = [primal_whole / norm_site]
    tangents_whole = [(tangent_whole - basis_whole[0] * norm_tangent) / norm_site]
    hess = jnp.zeros((KRYLOV, KRYLOV), jnp.float32)
    dhess = jnp.zeros((KRYLOV, KRYLOV), jnp.float32)
    gram = jnp.zeros((KRYLOV, KRYLOV), jnp.float32)
    cross = jnp.zeros((KRYLOV, KRYLOV), jnp.float32)
    for level in range(KRYLOV):
        both = apply(
            jnp.stack([basis[level], tangents[level]], axis=1),
            jnp.stack([basis_whole[level], tangents_whole[level]], axis=1),
        )
        image = both[:, 0]
        dimage = both[:, 1]
        if level + 1 < KRYLOV:
            both_whole = lax.all_gather(both, "row", axis=0, tiled=True)
            image_whole = both_whole[:, 0]
            dimage_whole = both_whole[:, 1]
        counted = level + 1
        locals_list = [inner(vector, image) for vector in basis]
        locals_list = locals_list + [inner(vector, image) for vector in tangents]
        locals_list = locals_list + [inner(vector, dimage) for vector in basis]
        last = level + 1 == KRYLOV
        if not last:
            newest = basis[level]
            locals_list = locals_list + [inner(image, image), inner(image, dimage)]
            locals_list = locals_list + [inner(newest, vector) for vector in basis]
            locals_list = locals_list + [inner(newest, vector) for vector in tangents]
            locals_list = locals_list + [inner(vector, tangents[level]) for vector in basis[:level]]
        totals = total(jnp.stack(locals_list))
        coeffs = totals[:counted]
        across = totals[counted : 2 * counted]
        along = totals[2 * counted : 3 * counted]
        dcoeffs = across + along
        hess = hess.at[:counted, level].set(coeffs)
        dhess = dhess.at[:counted, level].set(dcoeffs)
        if not last:
            at = 3 * counted
            squared_image = totals[at]
            image_dimage = totals[at + 1]
            at += 2
            gram = gram.at[level, :counted].set(totals[at : at + counted])
            gram = gram.at[:counted, level].set(totals[at : at + counted])
            at += counted
            cross = cross.at[level, :counted].set(totals[at : at + counted])
            at += counted
            cross = cross.at[:level, level].set(totals[at : at + level])
            g = gram[:counted, :counted]
            t = cross[:counted, :counted]
            squared = (
                squared_image
                - 2.0 * jnp.sum(coeffs * coeffs)
                + jnp.dot(coeffs, jnp.dot(g, coeffs, precision=lax.Precision.HIGHEST), precision=lax.Precision.HIGHEST)
            )
            mixed_term = (
                image_dimage
                - jnp.sum(dcoeffs * coeffs)
                - jnp.sum(coeffs * across)
                - jnp.sum(coeffs * along)
                + jnp.dot(coeffs, jnp.dot(g, dcoeffs, precision=lax.Precision.HIGHEST), precision=lax.Precision.HIGHEST)
                + jnp.dot(coeffs, jnp.dot(t, coeffs, precision=lax.Precision.HIGHEST), precision=lax.Precision.HIGHEST)
            )
            residual = image
            dresidual = dimage
            for index in range(counted):
                residual = residual - coeffs[index] * basis[index]
                dresidual = (
                    dresidual - dcoeffs[index] * basis[index] - coeffs[index] * tangents[index]
                )
            height = jnp.sqrt(squared)
            dheight = mixed_term / height
            newvec = residual / height
            basis.append(newvec)
            tangents.append((dresidual - newvec * dheight) / height)
            residual_whole = image_whole
            dresidual_whole = dimage_whole
            for index in range(counted):
                residual_whole = residual_whole - coeffs[index] * basis_whole[index]
                dresidual_whole = (
                    dresidual_whole
                    - dcoeffs[index] * basis_whole[index]
                    - coeffs[index] * tangents_whole[index]
                )
            newvec_whole = residual_whole / height
            basis_whole.append(newvec_whole)
            tangents_whole.append((dresidual_whole - newvec_whole * dheight) / height)
            hess = hess.at[level + 1, level].set(height)
            dhess = dhess.at[level + 1, level].set(dheight)
    coeff, dcoeff = taylor(hess, dhess)
    spread = jnp.zeros_like(primal)
    dspread = jnp.zeros_like(primal)
    for index in range(KRYLOV):
        spread = spread + coeff[index] * basis[index]
        dspread = dspread + coeff[index] * tangents[index] + dcoeff[index] * basis[index]
    evolved = norm_site * spread
    evolved_tangent = norm_tangent * spread + norm_site * dspread
    return (evolved, evolved_tangent)


def solution(mesh):
    in_specs = (
        P("row", None, "col"),
        P("row", None, "col"),
        P("row", "col"),
        P("row", "col"),
        P(),
        P(),
    )
    out_specs = (P("row", None, "col"), P("row", None, "col"))
    return jax.shard_map(local, mesh=mesh, in_specs=in_specs, out_specs=out_specs, check_vma=False)
```

```python
import jax
import jax.numpy as jnp
from jax import lax
from jax.sharding import PartitionSpec as P

KRYLOV = 3


taylor_order = 16


def inner(first, second):
    return jnp.sum(first * second)


def exchange_sum(values, axis):
    size = lax.psum(1, axis)
    copies = jnp.broadcast_to(values[None], (size,) + values.shape)
    return jnp.sum(lax.all_to_all(copies, axis, 0, 0, tiled=False), axis=0)


def total(values):
    return exchange_sum(exchange_sum(values, "col"), "row")


def taylor(hess, dhess):
    size = hess.shape[0]
    term = jnp.zeros((size,), jnp.float32).at[0].set(1.0)
    dterm = jnp.zeros((size,), jnp.float32)
    total = term
    dtotal = dterm
    for order in range(1, taylor_order + 1):
        nterm = jnp.dot(hess, term, precision=lax.Precision.HIGHEST) / order
        dterm = (
            jnp.dot(dhess, term, precision=lax.Precision.HIGHEST)
            + jnp.dot(hess, dterm, precision=lax.Precision.HIGHEST)
        ) / order
        term = nterm
        total = total + term
        dtotal = dtotal + dterm
    return (total, dtotal)


def local(site_tensor, site_tangent, left_env, right_env, mpo, dissipation):
    rows_here, physical, cols_here = site_tensor.shape
    channels = mpo.shape[0]
    left_whole = lax.all_gather(left_env, "col", axis=1, tiled=True)
    right_whole = lax.all_gather(right_env, "row", axis=0, tiled=True)
    right_whole = jnp.transpose(
        right_whole.reshape(right_whole.shape[0], cols_here, channels), (0, 2, 1)
    ).reshape(right_whole.shape[0], channels * cols_here)

    def apply(stacked, whole_stacked):
        panels = stacked.shape[1]
        whole = whole_stacked.astype(jnp.bfloat16)
        flat = whole.reshape(whole.shape[0], panels * physical * cols_here)
        left_three = left_whole.reshape(rows_here, flat.shape[0], channels)
        mixed = lax.dot_general(
            left_three, flat, (((1,), (0,)), ((), ())), preferred_element_type=jnp.float32
        )
        mixed = mixed.astype(jnp.bfloat16).reshape(rows_here, channels, panels, physical, cols_here)
        channel = jnp.einsum("awspr,wvpq->asqvr", mixed, mpo, preferred_element_type=jnp.float32)
        channel = channel.astype(jnp.bfloat16).reshape(
            rows_here * panels * physical, cols_here * channels
        )
        partial_cols = lax.dot_general(
            right_whole, channel, (((1,), (1,)), ((), ())), preferred_element_type=jnp.float32
        )
        blocks = lax.psum(1, "col")
        split = partial_cols.reshape(blocks, partial_cols.shape[0] // blocks, channel.shape[0])
        gathered = lax.all_to_all(split, "col", 0, 0, tiled=False)
        summed = jnp.sum(gathered, axis=0).reshape(cols_here, rows_here, panels, physical)
        summed = jnp.transpose(summed, (1, 2, 3, 0))
        return summed - dissipation[None, None, :, None] * stacked

    primal = site_tensor.astype(jnp.float32)
    tangent = site_tangent.astype(jnp.float32)
    starting = total(jnp.stack([inner(primal, primal), inner(primal, tangent)]))
    norm_site = jnp.sqrt(starting[0])
    norm_tangent = starting[1] / norm_site
    basis = [primal / norm_site]
    tangents = [(tangent - basis[0] * norm_tangent) / norm_site]
    inputs_whole = lax.all_gather(
        jnp.stack([site_tensor, site_tangent], axis=1), "row", axis=0, tiled=True
    ).astype(jnp.float32)
    primal_whole = inputs_whole[:, 0]
    tangent_whole = inputs_whole[:, 1]
    basis_whole = [primal_whole / norm_site]
    tangents_whole = [(tangent_whole - basis_whole[0] * norm_tangent) / norm_site]
    hess = jnp.zeros((KRYLOV, KRYLOV), jnp.float32)
    dhess = jnp.zeros((KRYLOV, KRYLOV), jnp.float32)
    gram = jnp.zeros((KRYLOV, KRYLOV), jnp.float32)
    cross = jnp.zeros((KRYLOV, KRYLOV), jnp.float32)
    for level in range(KRYLOV):
        both = apply(
            jnp.stack([basis[level], tangents[level]], axis=1),
            jnp.stack([basis_whole[level], tangents_whole[level]], axis=1),
        )
        image = both[:, 0]
        dimage = both[:, 1]
        if level + 1 < KRYLOV:
            both_whole = lax.all_gather(both, "row", axis=0, tiled=True)
            image_whole = both_whole[:, 0]
            dimage_whole = both_whole[:, 1]
        counted = level + 1
        locals_list = [inner(vector, image) for vector in basis]
        locals_list = locals_list + [inner(vector, image) for vector in tangents]
        locals_list = locals_list + [inner(vector, dimage) for vector in basis]
        last = level + 1 == KRYLOV
        if not last:
            newest = basis[level]
            locals_list = locals_list + [inner(image, image), inner(image, dimage)]
            locals_list = locals_list + [inner(newest, vector) for vector in basis]
            locals_list = locals_list + [inner(newest, vector) for vector in tangents]
            locals_list = locals_list + [inner(vector, tangents[level]) for vector in basis[:level]]
        totals = total(jnp.stack(locals_list))
        coeffs = totals[:counted]
        across = totals[counted : 2 * counted]
        along = totals[2 * counted : 3 * counted]
        dcoeffs = across + along
        hess = hess.at[:counted, level].set(coeffs)
        dhess = dhess.at[:counted, level].set(dcoeffs)
        if not last:
            at = 3 * counted
            squared_image = totals[at]
            image_dimage = totals[at + 1]
            at += 2
            gram = gram.at[level, :counted].set(totals[at : at + counted])
            gram = gram.at[:counted, level].set(totals[at : at + counted])
            at += counted
            cross = cross.at[level, :counted].set(totals[at : at + counted])
            at += counted
            cross = cross.at[:level, level].set(totals[at : at + level])
            g = gram[:counted, :counted]
            t = cross[:counted, :counted]
            squared = (
                squared_image
                - 2.0 * jnp.sum(coeffs * coeffs)
                + jnp.dot(coeffs, jnp.dot(g, coeffs, precision=lax.Precision.HIGHEST), precision=lax.Precision.HIGHEST)
            )
            mixed_term = (
                image_dimage
                - jnp.sum(dcoeffs * coeffs)
                - jnp.sum(coeffs * across)
                - jnp.sum(coeffs * along)
                + jnp.dot(coeffs, jnp.dot(g, dcoeffs, precision=lax.Precision.HIGHEST), precision=lax.Precision.HIGHEST)
                + jnp.dot(coeffs, jnp.dot(t, coeffs, precision=lax.Precision.HIGHEST), precision=lax.Precision.HIGHEST)
            )
            residual = image
            dresidual = dimage
            for index in range(counted):
                residual = residual - coeffs[index] * basis[index]
                dresidual = (
                    dresidual - dcoeffs[index] * basis[index] - coeffs[index] * tangents[index]
                )
            height = jnp.sqrt(squared)
            dheight = mixed_term / height
            newvec = residual / height
            basis.append(newvec)
            tangents.append((dresidual - newvec * dheight) / height)
            residual_whole = image_whole
            dresidual_whole = dimage_whole
            for index in range(counted):
                residual_whole = residual_whole - coeffs[index] * basis_whole[index]
                dresidual_whole = (
                    dresidual_whole
                    - dcoeffs[index] * basis_whole[index]
                    - coeffs[index] * tangents_whole[index]
                )
            newvec_whole = residual_whole / height
            basis_whole.append(newvec_whole)
            tangents_whole.append((dresidual_whole - newvec_whole * dheight) / height)
            hess = hess.at[level + 1, level].set(height)
            dhess = dhess.at[level + 1, level].set(dheight)
    coeff, dcoeff = taylor(hess, dhess)
    spread = jnp.zeros_like(primal)
    dspread = jnp.zeros_like(primal)
    for index in range(KRYLOV):
        spread = spread + coeff[index] * basis[index]
        dspread = dspread + coeff[index] * tangents[index] + dcoeff[index] * basis[index]
    evolved = norm_site * spread
    evolved_tangent = norm_tangent * spread + norm_site * dspread
    return (evolved, evolved_tangent)


def solution(mesh):
    in_specs = (
        P("row", None, "col"),
        P("row", None, "col"),
        P("row", "col"),
        P("row", "col"),
        P(),
        P(),
    )
    out_specs = (P("row", None, "col"), P("row", None, "col"))
    return jax.shard_map(local, mesh=mesh, in_specs=in_specs, out_specs=out_specs, check_vma=False)
```

```python
import jax
import jax.numpy as jnp
from jax import lax
from jax.sharding import PartitionSpec as P

KRYLOV = 3


taylor_order = 16


def inner(first, second):
    return jnp.sum(first * second)


def exchange_sum(values, axis):
    size = lax.psum(1, axis)
    copies = jnp.broadcast_to(values[None], (size,) + values.shape)
    return jnp.sum(lax.all_to_all(copies, axis, 0, 0, tiled=False), axis=0)


def gather_by_exchange(values, axis):
    size = lax.psum(1, axis)
    copies = jnp.broadcast_to(values[None], (size,) + values.shape)
    return lax.all_to_all(copies, axis, 0, 0, tiled=False)


def total(values):
    return exchange_sum(exchange_sum(values, "col"), "row")


def taylor(hess, dhess):
    size = hess.shape[0]
    term = jnp.zeros((size,), jnp.float32).at[0].set(1.0)
    dterm = jnp.zeros((size,), jnp.float32)
    total = term
    dtotal = dterm
    for order in range(1, taylor_order + 1):
        nterm = jnp.dot(hess, term, precision=lax.Precision.HIGHEST) / order
        dterm = (
            jnp.dot(dhess, term, precision=lax.Precision.HIGHEST)
            + jnp.dot(hess, dterm, precision=lax.Precision.HIGHEST)
        ) / order
        term = nterm
        total = total + term
        dtotal = dtotal + dterm
    return (total, dtotal)


def local(site_tensor, site_tangent, left_env, right_env, mpo, dissipation):
    rows_here, physical, cols_here = site_tensor.shape
    channels = mpo.shape[0]
    left_blocks = gather_by_exchange(left_env, "col")
    left_whole = jnp.transpose(left_blocks, (1, 0, 2)).reshape(rows_here, -1)
    right_whole = lax.all_gather(right_env, "row", axis=0, tiled=True)
    right_whole = jnp.transpose(
        right_whole.reshape(right_whole.shape[0], cols_here, channels), (0, 2, 1)
    ).reshape(right_whole.shape[0], channels * cols_here)

    def apply(stacked, whole_stacked):
        panels = stacked.shape[1]
        whole = whole_stacked.astype(jnp.bfloat16)
        flat = whole.reshape(whole.shape[0], panels * physical * cols_here)
        left_three = left_whole.reshape(rows_here, flat.shape[0], channels)
        mixed = lax.dot_general(
            left_three, flat, (((1,), (0,)), ((), ())), preferred_element_type=jnp.float32
        )
        mixed = mixed.astype(jnp.bfloat16).reshape(rows_here, channels, panels, physical, cols_here)
        channel = jnp.einsum("awspr,wvpq->asqvr", mixed, mpo, preferred_element_type=jnp.float32)
        channel = channel.astype(jnp.bfloat16).reshape(
            rows_here * panels * physical, cols_here * channels
        )
        partial_cols = lax.dot_general(
            right_whole, channel, (((1,), (1,)), ((), ())), preferred_element_type=jnp.float32
        )
        blocks = lax.psum(1, "col")
        split = partial_cols.reshape(blocks, partial_cols.shape[0] // blocks, channel.shape[0])
        gathered = lax.all_to_all(split, "col", 0, 0, tiled=False)
        summed = jnp.sum(gathered, axis=0).reshape(cols_here, rows_here, panels, physical)
        summed = jnp.transpose(summed, (1, 2, 3, 0))
        return summed - dissipation[None, None, :, None] * stacked

    primal = site_tensor.astype(jnp.float32)
    tangent = site_tangent.astype(jnp.float32)
    starting = total(jnp.stack([inner(primal, primal), inner(primal, tangent)]))
    norm_site = jnp.sqrt(starting[0])
    norm_tangent = starting[1] / norm_site
    basis = [primal / norm_site]
    tangents = [(tangent - basis[0] * norm_tangent) / norm_site]
    inputs_blocks = gather_by_exchange(jnp.stack([site_tensor, site_tangent], axis=1), "row")
    inputs_whole = inputs_blocks.reshape((-1,) + inputs_blocks.shape[2:]).astype(jnp.float32)
    primal_whole = inputs_whole[:, 0]
    tangent_whole = inputs_whole[:, 1]
    basis_whole = [primal_whole / norm_site]
    tangents_whole = [(tangent_whole - basis_whole[0] * norm_tangent) / norm_site]
    hess = jnp.zeros((KRYLOV, KRYLOV), jnp.float32)
    dhess = jnp.zeros((KRYLOV, KRYLOV), jnp.float32)
    gram = jnp.zeros((KRYLOV, KRYLOV), jnp.float32)
    cross = jnp.zeros((KRYLOV, KRYLOV), jnp.float32)
    for level in range(KRYLOV):
        both = apply(
            jnp.stack([basis[level], tangents[level]], axis=1),
            jnp.stack([basis_whole[level], tangents_whole[level]], axis=1),
        )
        image = both[:, 0]
        dimage = both[:, 1]
        if level + 1 < KRYLOV:
            both_whole = lax.all_gather(both, "row", axis=0, tiled=True)
            image_whole = both_whole[:, 0]
            dimage_whole = both_whole[:, 1]
        counted = level + 1
        locals_list = [inner(vector, image) for vector in basis]
        locals_list = locals_list + [inner(vector, image) for vector in tangents]
        locals_list = locals_list + [inner(vector, dimage) for vector in basis]
        last = level + 1 == KRYLOV
        if not last:
            newest = basis[level]
            locals_list = locals_list + [inner(image, image), inner(image, dimage)]
            locals_list = locals_list + [inner(newest, vector) for vector in basis]
            locals_list = locals_list + [inner(newest, vector) for vector in tangents]
            locals_list = locals_list + [inner(vector, tangents[level]) for vector in basis[:level]]
        totals = total(jnp.stack(locals_list))
        coeffs = totals[:counted]
        across = totals[counted : 2 * counted]
        along = totals[2 * counted : 3 * counted]
        dcoeffs = across + along
        hess = hess.at[:counted, level].set(coeffs)
        dhess = dhess.at[:counted, level].set(dcoeffs)
        if not last:
            at = 3 * counted
            squared_image = totals[at]
            image_dimage = totals[at + 1]
            at += 2
            gram = gram.at[level, :counted].set(totals[at : at + counted])
            gram = gram.at[:counted, level].set(totals[at : at + counted])
            at += counted
            cross = cross.at[level, :counted].set(totals[at : at + counted])
            at += counted
            cross = cross.at[:level, level].set(totals[at : at + level])
            g = gram[:counted, :counted]
            t = cross[:counted, :counted]
            squared = (
                squared_image
                - 2.0 * jnp.sum(coeffs * coeffs)
                + jnp.dot(coeffs, jnp.dot(g, coeffs, precision=lax.Precision.HIGHEST), precision=lax.Precision.HIGHEST)
            )
            mixed_term = (
                image_dimage
                - jnp.sum(dcoeffs * coeffs)
                - jnp.sum(coeffs * across)
                - jnp.sum(coeffs * along)
                + jnp.dot(coeffs, jnp.dot(g, dcoeffs, precision=lax.Precision.HIGHEST), precision=lax.Precision.HIGHEST)
                + jnp.dot(coeffs, jnp.dot(t, coeffs, precision=lax.Precision.HIGHEST), precision=lax.Precision.HIGHEST)
            )
            residual = image
            dresidual = dimage
            for index in range(counted):
                residual = residual - coeffs[index] * basis[index]
                dresidual = (
                    dresidual - dcoeffs[index] * basis[index] - coeffs[index] * tangents[index]
                )
            height = jnp.sqrt(squared)
            dheight = mixed_term / height
            newvec = residual / height
            basis.append(newvec)
            tangents.append((dresidual - newvec * dheight) / height)
            residual_whole = image_whole
            dresidual_whole = dimage_whole
            for index in range(counted):
                residual_whole = residual_whole - coeffs[index] * basis_whole[index]
                dresidual_whole = (
                    dresidual_whole
                    - dcoeffs[index] * basis_whole[index]
                    - coeffs[index] * tangents_whole[index]
                )
            newvec_whole = residual_whole / height
            basis_whole.append(newvec_whole)
            tangents_whole.append((dresidual_whole - newvec_whole * dheight) / height)
            hess = hess.at[level + 1, level].set(height)
            dhess = dhess.at[level + 1, level].set(dheight)
    coeff, dcoeff = taylor(hess, dhess)
    spread = jnp.zeros_like(primal)
    dspread = jnp.zeros_like(primal)
    for index in range(KRYLOV):
        spread = spread + coeff[index] * basis[index]
        dspread = dspread + coeff[index] * tangents[index] + dcoeff[index] * basis[index]
    evolved = norm_site * spread
    evolved_tangent = norm_tangent * spread + norm_site * dspread
    return (evolved, evolved_tangent)


def solution(mesh):
    in_specs = (
        P("row", None, "col"),
        P("row", None, "col"),
        P("row", "col"),
        P("row", "col"),
        P(),
        P(),
    )
    out_specs = (P("row", None, "col"), P("row", None, "col"))
    return jax.shard_map(local, mesh=mesh, in_specs=in_specs, out_specs=out_specs, check_vma=False)
```

```python
import jax
import jax.numpy as jnp
from jax import lax
from jax.sharding import PartitionSpec as P

KRYLOV = 3


taylor_order = 16


def inner(first, second):
    return jnp.sum(first * second)


def exchange_sum(values, axis):
    size = lax.psum(1, axis)
    copies = jnp.broadcast_to(values[None], (size,) + values.shape)
    return jnp.sum(lax.all_to_all(copies, axis, 0, 0, tiled=False), axis=0)


def gather_by_exchange(values, axis):
    size = lax.psum(1, axis)
    copies = jnp.broadcast_to(values[None], (size,) + values.shape)
    return lax.all_to_all(copies, axis, 0, 0, tiled=False)


def total(values):
    return exchange_sum(exchange_sum(values, "col"), "row")


def taylor(hess, dhess):
    size = hess.shape[0]
    term = jnp.zeros((size,), jnp.float32).at[0].set(1.0)
    dterm = jnp.zeros((size,), jnp.float32)
    total = term
    dtotal = dterm
    for order in range(1, taylor_order + 1):
        nterm = jnp.dot(hess, term, precision=lax.Precision.HIGHEST) / order
        dterm = (
            jnp.dot(dhess, term, precision=lax.Precision.HIGHEST)
            + jnp.dot(hess, dterm, precision=lax.Precision.HIGHEST)
        ) / order
        term = nterm
        total = total + term
        dtotal = dtotal + dterm
    return (total, dtotal)


def local(site_tensor, site_tangent, left_env, right_env, mpo, dissipation):
    rows_here, physical, cols_here = site_tensor.shape
    channels = mpo.shape[0]
    left_blocks = gather_by_exchange(left_env, "col")
    left_whole = jnp.transpose(left_blocks, (1, 0, 2)).reshape(rows_here, -1)
    right_whole = lax.all_gather(right_env, "row", axis=0, tiled=True)
    right_whole = jnp.transpose(
        right_whole.reshape(right_whole.shape[0], cols_here, channels), (0, 2, 1)
    ).reshape(right_whole.shape[0], channels * cols_here)

    def apply(stacked, whole_stacked):
        panels = stacked.shape[1]
        whole = whole_stacked.astype(jnp.bfloat16)
        flat = whole.reshape(whole.shape[0], panels * physical * cols_here)
        left_three = left_whole.reshape(rows_here, flat.shape[0], channels)
        mixed = lax.dot_general(
            left_three, flat, (((1,), (0,)), ((), ())), preferred_element_type=jnp.float32
        )
        mixed = mixed.astype(jnp.bfloat16).reshape(rows_here, channels, panels, physical, cols_here)
        channel = jnp.einsum("awspr,wvpq->asqvr", mixed, mpo, preferred_element_type=jnp.float32)
        channel = channel.astype(jnp.bfloat16).reshape(
            rows_here * panels * physical, cols_here * channels
        )
        partial_cols = lax.dot_general(
            right_whole, channel, (((1,), (1,)), ((), ())), preferred_element_type=jnp.float32
        )
        blocks = lax.psum(1, "col")
        split = partial_cols.reshape(blocks, partial_cols.shape[0] // blocks, channel.shape[0])
        gathered = lax.all_to_all(split, "col", 0, 0, tiled=False)
        summed = jnp.sum(gathered, axis=0).reshape(cols_here, rows_here, panels, physical)
        summed = jnp.transpose(summed, (1, 2, 3, 0))
        return summed - dissipation[None, None, :, None] * stacked

    primal = site_tensor.astype(jnp.float32)
    tangent = site_tangent.astype(jnp.float32)
    starting = total(jnp.stack([inner(primal, primal), inner(primal, tangent)]))
    norm_site = jnp.sqrt(starting[0])
    norm_tangent = starting[1] / norm_site
    basis = [primal / norm_site]
    tangents = [(tangent - basis[0] * norm_tangent) / norm_site]
    inputs_whole = lax.all_gather(
        jnp.stack([site_tensor, site_tangent], axis=1), "row", axis=0, tiled=True
    ).astype(jnp.float32)
    primal_whole = inputs_whole[:, 0]
    tangent_whole = inputs_whole[:, 1]
    basis_whole = [primal_whole / norm_site]
    tangents_whole = [(tangent_whole - basis_whole[0] * norm_tangent) / norm_site]
    hess = jnp.zeros((KRYLOV, KRYLOV), jnp.float32)
    dhess = jnp.zeros((KRYLOV, KRYLOV), jnp.float32)
    gram = jnp.zeros((KRYLOV, KRYLOV), jnp.float32)
    cross = jnp.zeros((KRYLOV, KRYLOV), jnp.float32)
    for level in range(KRYLOV):
        both = apply(
            jnp.stack([basis[level], tangents[level]], axis=1),
            jnp.stack([basis_whole[level], tangents_whole[level]], axis=1),
        )
        image = both[:, 0]
        dimage = both[:, 1]
        if level + 1 < KRYLOV:
            both_whole = lax.all_gather(both, "row", axis=0, tiled=True)
            image_whole = both_whole[:, 0]
            dimage_whole = both_whole[:, 1]
        counted = level + 1
        locals_list = [inner(vector, image) for vector in basis]
        locals_list = locals_list + [inner(vector, image) for vector in tangents]
        locals_list = locals_list + [inner(vector, dimage) for vector in basis]
        last = level + 1 == KRYLOV
        if not last:
            newest = basis[level]
            locals_list = locals_list + [inner(image, image), inner(image, dimage)]
            locals_list = locals_list + [inner(newest, vector) for vector in basis]
            locals_list = locals_list + [inner(newest, vector) for vector in tangents]
            locals_list = locals_list + [inner(vector, tangents[level]) for vector in basis[:level]]
        totals = total(jnp.stack(locals_list))
        coeffs = totals[:counted]
        across = totals[counted : 2 * counted]
        along = totals[2 * counted : 3 * counted]
        dcoeffs = across + along
        hess = hess.at[:counted, level].set(coeffs)
        dhess = dhess.at[:counted, level].set(dcoeffs)
        if not last:
            at = 3 * counted
            squared_image = totals[at]
            image_dimage = totals[at + 1]
            at += 2
            gram = gram.at[level, :counted].set(totals[at : at + counted])
            gram = gram.at[:counted, level].set(totals[at : at + counted])
            at += counted
            cross = cross.at[level, :counted].set(totals[at : at + counted])
            at += counted
            cross = cross.at[:level, level].set(totals[at : at + level])
            g = gram[:counted, :counted]
            t = cross[:counted, :counted]
            squared = (
                squared_image
                - 2.0 * jnp.sum(coeffs * coeffs)
                + jnp.dot(coeffs, jnp.dot(g, coeffs, precision=lax.Precision.HIGHEST), precision=lax.Precision.HIGHEST)
            )
            mixed_term = (
                image_dimage
                - jnp.sum(dcoeffs * coeffs)
                - jnp.sum(coeffs * across)
                - jnp.sum(coeffs * along)
                + jnp.dot(coeffs, jnp.dot(g, dcoeffs, precision=lax.Precision.HIGHEST), precision=lax.Precision.HIGHEST)
                + jnp.dot(coeffs, jnp.dot(t, coeffs, precision=lax.Precision.HIGHEST), precision=lax.Precision.HIGHEST)
            )
            residual = image
            dresidual = dimage
            for index in range(counted):
                residual = residual - coeffs[index] * basis[index]
                dresidual = (
                    dresidual - dcoeffs[index] * basis[index] - coeffs[index] * tangents[index]
                )
            height = jnp.sqrt(squared)
            dheight = mixed_term / height
            newvec = residual / height
            basis.append(newvec)
            tangents.append((dresidual - newvec * dheight) / height)
            residual_whole = image_whole
            dresidual_whole = dimage_whole
            for index in range(counted):
                residual_whole = residual_whole - coeffs[index] * basis_whole[index]
                dresidual_whole = (
                    dresidual_whole
                    - dcoeffs[index] * basis_whole[index]
                    - coeffs[index] * tangents_whole[index]
                )
            newvec_whole = residual_whole / height
            basis_whole.append(newvec_whole)
            tangents_whole.append((dresidual_whole - newvec_whole * dheight) / height)
            hess = hess.at[level + 1, level].set(height)
            dhess = dhess.at[level + 1, level].set(dheight)
    coeff, dcoeff = taylor(hess, dhess)
    spread = jnp.zeros_like(primal)
    dspread = jnp.zeros_like(primal)
    for index in range(KRYLOV):
        spread = spread + coeff[index] * basis[index]
        dspread = dspread + coeff[index] * tangents[index] + dcoeff[index] * basis[index]
    evolved = norm_site * spread
    evolved_tangent = norm_tangent * spread + norm_site * dspread
    return (evolved, evolved_tangent)


def solution(mesh):
    in_specs = (
        P("row", None, "col"),
        P("row", None, "col"),
        P("row", "col"),
        P("row", "col"),
        P(),
        P(),
    )
    out_specs = (P("row", None, "col"), P("row", None, "col"))
    return jax.shard_map(local, mesh=mesh, in_specs=in_specs, out_specs=out_specs, check_vma=False)
```

```python
import jax
import jax.numpy as jnp
from jax import lax
from jax.sharding import PartitionSpec as P

KRYLOV = 3


taylor_order = 16


def inner(first, second):
    return jnp.sum(first * second)


def exchange_sum(values, axis):
    size = lax.psum(1, axis)
    copies = jnp.broadcast_to(values[None], (size,) + values.shape)
    return jnp.sum(lax.all_to_all(copies, axis, 0, 0, tiled=False), axis=0)


def gather_by_exchange(values, axis):
    size = lax.psum(1, axis)
    copies = jnp.broadcast_to(values[None], (size,) + values.shape)
    return lax.all_to_all(copies, axis, 0, 0, tiled=False)


def total(values):
    return exchange_sum(exchange_sum(values, "col"), "row")


def taylor(hess, dhess):
    size = hess.shape[0]
    term = jnp.zeros((size,), jnp.float32).at[0].set(1.0)
    dterm = jnp.zeros((size,), jnp.float32)
    total = term
    dtotal = dterm
    for order in range(1, taylor_order + 1):
        nterm = jnp.dot(hess, term, precision=lax.Precision.HIGHEST) / order
        dterm = (
            jnp.dot(dhess, term, precision=lax.Precision.HIGHEST)
            + jnp.dot(hess, dterm, precision=lax.Precision.HIGHEST)
        ) / order
        term = nterm
        total = total + term
        dtotal = dtotal + dterm
    return (total, dtotal)


def local(site_tensor, site_tangent, left_env, right_env, mpo, dissipation):
    rows_here, physical, cols_here = site_tensor.shape
    channels = mpo.shape[0]
    left_blocks = gather_by_exchange(left_env, "col")
    left_whole = jnp.transpose(left_blocks, (1, 0, 2)).reshape(rows_here, -1)
    right_whole = lax.all_gather(right_env, "row", axis=0, tiled=True)
    right_whole = jnp.transpose(
        right_whole.reshape(right_whole.shape[0], cols_here, channels), (0, 2, 1)
    ).reshape(right_whole.shape[0], channels * cols_here)

    def apply(stacked, whole_stacked):
        panels = stacked.shape[1]
        whole = whole_stacked.astype(jnp.bfloat16)
        flat = whole.reshape(whole.shape[0], panels * physical * cols_here)
        left_three = left_whole.reshape(rows_here, flat.shape[0], channels)
        mixed = lax.dot_general(
            left_three, flat, (((1,), (0,)), ((), ())), preferred_element_type=jnp.float32
        )
        mixed = mixed.astype(jnp.bfloat16).reshape(rows_here, channels, panels, physical, cols_here)
        channel = jnp.einsum("awspr,wvpq->asqvr", mixed, mpo, preferred_element_type=jnp.float32)
        channel = channel.astype(jnp.bfloat16).reshape(
            rows_here * panels * physical, cols_here * channels
        )
        partial_cols = lax.dot_general(
            right_whole, channel, (((1,), (1,)), ((), ())), preferred_element_type=jnp.float32
        )
        blocks = lax.psum(1, "col")
        split = partial_cols.reshape(blocks, partial_cols.shape[0] // blocks, channel.shape[0])
        gathered = lax.all_to_all(split, "col", 0, 0, tiled=False)
        summed = jnp.sum(gathered, axis=0).reshape(cols_here, rows_here, panels, physical)
        summed = jnp.transpose(summed, (1, 2, 3, 0))
        return summed - dissipation[None, None, :, None] * stacked

    primal = site_tensor.astype(jnp.float32)
    tangent = site_tangent.astype(jnp.float32)
    starting = total(jnp.stack([inner(primal, primal), inner(primal, tangent)]))
    norm_site = jnp.sqrt(starting[0])
    norm_tangent = starting[1] / norm_site
    basis = [primal / norm_site]
    tangents = [(tangent - basis[0] * norm_tangent) / norm_site]
    inputs_whole = lax.all_gather(
        jnp.stack([site_tensor, site_tangent], axis=1), "row", axis=0, tiled=True
    ).astype(jnp.float32)
    primal_whole = inputs_whole[:, 0]
    tangent_whole = inputs_whole[:, 1]
    basis_whole = [primal_whole / norm_site]
    tangents_whole = [(tangent_whole - basis_whole[0] * norm_tangent) / norm_site]
    hess = jnp.zeros((KRYLOV, KRYLOV), jnp.float32)
    dhess = jnp.zeros((KRYLOV, KRYLOV), jnp.float32)
    gram = jnp.zeros((KRYLOV, KRYLOV), jnp.float32)
    cross = jnp.zeros((KRYLOV, KRYLOV), jnp.float32)
    for level in range(KRYLOV):
        both = apply(
            jnp.stack([basis[level], tangents[level]], axis=1),
            jnp.stack([basis_whole[level], tangents_whole[level]], axis=1),
        )
        image = both[:, 0]
        dimage = both[:, 1]
        if level + 1 < KRYLOV:
            both_whole = lax.all_gather(both, "row", axis=0, tiled=True)
            image_whole = both_whole[:, 0]
            dimage_whole = both_whole[:, 1]
        counted = level + 1
        vectors = jnp.stack(basis + tangents + [image, dimage]).reshape(2 * counted + 2, -1)
        products = lax.dot_general(
            vectors,
            vectors,
            (((1,), (1,)), ((), ())),
            precision=lax.Precision.HIGHEST,
            preferred_element_type=jnp.float32,
        )
        sums = total(products.reshape(-1)).reshape(products.shape)
        at_image = 2 * counted
        coeffs = sums[:counted, at_image]
        across = sums[counted : 2 * counted, at_image]
        along = sums[:counted, at_image + 1]
        dcoeffs = across + along
        hess = hess.at[:counted, level].set(coeffs)
        dhess = dhess.at[:counted, level].set(dcoeffs)
        last = level + 1 == KRYLOV
        if not last:
            squared_image = sums[at_image, at_image]
            image_dimage = sums[at_image, at_image + 1]
            gram = gram.at[:counted, :counted].set(sums[:counted, :counted])
            cross = cross.at[:counted, :counted].set(sums[:counted, counted : 2 * counted])
            g = gram[:counted, :counted]
            t = cross[:counted, :counted]
            squared = (
                squared_image
                - 2.0 * jnp.sum(coeffs * coeffs)
                + jnp.dot(coeffs, jnp.dot(g, coeffs, precision=lax.Precision.HIGHEST), precision=lax.Precision.HIGHEST)
            )
            mixed_term = (
                image_dimage
                - jnp.sum(dcoeffs * coeffs)
                - jnp.sum(coeffs * across)
                - jnp.sum(coeffs * along)
                + jnp.dot(coeffs, jnp.dot(g, dcoeffs, precision=lax.Precision.HIGHEST), precision=lax.Precision.HIGHEST)
                + jnp.dot(coeffs, jnp.dot(t, coeffs, precision=lax.Precision.HIGHEST), precision=lax.Precision.HIGHEST)
            )
            residual = image
            dresidual = dimage
            for index in range(counted):
                residual = residual - coeffs[index] * basis[index]
                dresidual = (
                    dresidual - dcoeffs[index] * basis[index] - coeffs[index] * tangents[index]
                )
            height = jnp.sqrt(squared)
            dheight = mixed_term / height
            newvec = residual / height
            basis.append(newvec)
            tangents.append((dresidual - newvec * dheight) / height)
            residual_whole = image_whole
            dresidual_whole = dimage_whole
            for index in range(counted):
                residual_whole = residual_whole - coeffs[index] * basis_whole[index]
                dresidual_whole = (
                    dresidual_whole
                    - dcoeffs[index] * basis_whole[index]
                    - coeffs[index] * tangents_whole[index]
                )
            newvec_whole = residual_whole / height
            basis_whole.append(newvec_whole)
            tangents_whole.append((dresidual_whole - newvec_whole * dheight) / height)
            hess = hess.at[level + 1, level].set(height)
            dhess = dhess.at[level + 1, level].set(dheight)
    coeff, dcoeff = taylor(hess, dhess)
    spread = jnp.zeros_like(primal)
    dspread = jnp.zeros_like(primal)
    for index in range(KRYLOV):
        spread = spread + coeff[index] * basis[index]
        dspread = dspread + coeff[index] * tangents[index] + dcoeff[index] * basis[index]
    evolved = norm_site * spread
    evolved_tangent = norm_tangent * spread + norm_site * dspread
    return (evolved, evolved_tangent)


def solution(mesh):
    in_specs = (
        P("row", None, "col"),
        P("row", None, "col"),
        P("row", "col"),
        P("row", "col"),
        P(),
        P(),
    )
    out_specs = (P("row", None, "col"), P("row", None, "col"))
    return jax.shard_map(local, mesh=mesh, in_specs=in_specs, out_specs=out_specs, check_vma=False)
```

```python
import jax
import jax.numpy as jnp
from jax import lax
from jax.sharding import PartitionSpec as P

KRYLOV = 3


taylor_order = 16


def inner(first, second):
    return jnp.sum(first * second)


def exchange_sum(values, axis):
    size = lax.psum(1, axis)
    copies = jnp.broadcast_to(values[None], (size,) + values.shape)
    return jnp.sum(lax.all_to_all(copies, axis, 0, 0, tiled=False), axis=0)


def gather_by_exchange(values, axis):
    size = lax.psum(1, axis)
    copies = jnp.broadcast_to(values[None], (size,) + values.shape)
    return lax.all_to_all(copies, axis, 0, 0, tiled=False)


def total(values):
    return exchange_sum(exchange_sum(values, "col"), "row")


def taylor(hess, dhess):
    size = hess.shape[0]
    term = jnp.zeros((size,), jnp.float32).at[0].set(1.0)
    dterm = jnp.zeros((size,), jnp.float32)
    total = term
    dtotal = dterm
    for order in range(1, taylor_order + 1):
        nterm = jnp.dot(hess, term, precision=lax.Precision.HIGHEST) / order
        dterm = (
            jnp.dot(dhess, term, precision=lax.Precision.HIGHEST)
            + jnp.dot(hess, dterm, precision=lax.Precision.HIGHEST)
        ) / order
        term = nterm
        total = total + term
        dtotal = dtotal + dterm
    return (total, dtotal)


def local(site_tensor, site_tangent, left_env, right_env, mpo, dissipation):
    rows_here, physical, cols_here = site_tensor.shape
    channels = mpo.shape[0]
    left_blocks = gather_by_exchange(left_env, "col")
    left_whole = jnp.transpose(left_blocks, (1, 0, 2)).reshape(rows_here, -1)
    right_whole = lax.all_gather(right_env, "row", axis=0, tiled=True)
    right_whole = jnp.transpose(
        right_whole.reshape(right_whole.shape[0], cols_here, channels), (0, 2, 1)
    ).reshape(right_whole.shape[0], channels * cols_here)

    def apply(stacked, whole_stacked):
        panels = stacked.shape[1]
        whole = whole_stacked.astype(jnp.bfloat16)
        flat = whole.reshape(whole.shape[0], panels * physical * cols_here)
        left_three = left_whole.reshape(rows_here, flat.shape[0], channels)
        mixed = lax.dot_general(
            left_three, flat, (((1,), (0,)), ((), ())), preferred_element_type=jnp.float32
        )
        mixed = mixed.astype(jnp.bfloat16).reshape(rows_here, channels, panels, physical, cols_here)
        channel = jnp.einsum("awspr,wvpq->asqvr", mixed, mpo, preferred_element_type=jnp.float32)
        channel = channel.astype(jnp.bfloat16).reshape(
            rows_here * panels * physical, cols_here * channels
        )
        partial_cols = lax.dot_general(
            right_whole, channel, (((1,), (1,)), ((), ())), preferred_element_type=jnp.float32
        )
        blocks = lax.psum(1, "col")
        split = partial_cols.reshape(blocks, partial_cols.shape[0] // blocks, channel.shape[0])
        gathered = lax.all_to_all(split, "col", 0, 0, tiled=False)
        summed = jnp.sum(gathered, axis=0).reshape(cols_here, rows_here, panels, physical)
        summed = jnp.transpose(summed, (2, 1, 3, 0))
        return summed - dissipation[None, None, :, None] * jnp.transpose(stacked, (1, 0, 2, 3))

    primal = site_tensor.astype(jnp.float32)
    tangent = site_tangent.astype(jnp.float32)
    starting = total(jnp.stack([inner(primal, primal), inner(primal, tangent)]))
    norm_site = jnp.sqrt(starting[0])
    norm_tangent = starting[1] / norm_site
    basis = [primal / norm_site]
    tangents = [(tangent - basis[0] * norm_tangent) / norm_site]
    inputs_whole = lax.all_gather(
        jnp.stack([site_tensor, site_tangent], axis=1), "row", axis=0, tiled=True
    ).astype(jnp.float32)
    primal_whole = inputs_whole[:, 0]
    tangent_whole = inputs_whole[:, 1]
    basis_whole = [primal_whole / norm_site]
    tangents_whole = [(tangent_whole - basis_whole[0] * norm_tangent) / norm_site]
    hess = jnp.zeros((KRYLOV, KRYLOV), jnp.float32)
    dhess = jnp.zeros((KRYLOV, KRYLOV), jnp.float32)
    gram = jnp.zeros((KRYLOV, KRYLOV), jnp.float32)
    cross = jnp.zeros((KRYLOV, KRYLOV), jnp.float32)
    for level in range(KRYLOV):
        both = apply(
            jnp.stack([basis[level], tangents[level]], axis=1),
            jnp.stack([basis_whole[level], tangents_whole[level]], axis=1),
        )
        image = both[0]
        dimage = both[1]
        if level + 1 < KRYLOV:
            both_whole = lax.all_gather(both, "row", axis=1, tiled=True)
            image_whole = both_whole[0]
            dimage_whole = both_whole[1]
        counted = level + 1
        vectors = jnp.stack(basis + tangents + [image, dimage]).reshape(2 * counted + 2, -1)
        products = lax.dot_general(
            vectors,
            vectors,
            (((1,), (1,)), ((), ())),
            precision=lax.Precision.HIGHEST,
            preferred_element_type=jnp.float32,
        )
        sums = total(products.reshape(-1)).reshape(products.shape)
        at_image = 2 * counted
        coeffs = sums[:counted, at_image]
        across = sums[counted : 2 * counted, at_image]
        along = sums[:counted, at_image + 1]
        dcoeffs = across + along
        hess = hess.at[:counted, level].set(coeffs)
        dhess = dhess.at[:counted, level].set(dcoeffs)
        last = level + 1 == KRYLOV
        if not last:
            squared_image = sums[at_image, at_image]
            image_dimage = sums[at_image, at_image + 1]
            gram = gram.at[:counted, :counted].set(sums[:counted, :counted])
            cross = cross.at[:counted, :counted].set(sums[:counted, counted : 2 * counted])
            g = gram[:counted, :counted]
            t = cross[:counted, :counted]
            squared = (
                squared_image
                - 2.0 * jnp.sum(coeffs * coeffs)
                + jnp.dot(coeffs, jnp.dot(g, coeffs, precision=lax.Precision.HIGHEST), precision=lax.Precision.HIGHEST)
            )
            mixed_term = (
                image_dimage
                - jnp.sum(dcoeffs * coeffs)
                - jnp.sum(coeffs * across)
                - jnp.sum(coeffs * along)
                + jnp.dot(coeffs, jnp.dot(g, dcoeffs, precision=lax.Precision.HIGHEST), precision=lax.Precision.HIGHEST)
                + jnp.dot(coeffs, jnp.dot(t, coeffs, precision=lax.Precision.HIGHEST), precision=lax.Precision.HIGHEST)
            )
            residual = image
            dresidual = dimage
            for index in range(counted):
                residual = residual - coeffs[index] * basis[index]
                dresidual = (
                    dresidual - dcoeffs[index] * basis[index] - coeffs[index] * tangents[index]
                )
            height = jnp.sqrt(squared)
            dheight = mixed_term / height
            newvec = residual / height
            basis.append(newvec)
            tangents.append((dresidual - newvec * dheight) / height)
            residual_whole = image_whole
            dresidual_whole = dimage_whole
            for index in range(counted):
                residual_whole = residual_whole - coeffs[index] * basis_whole[index]
                dresidual_whole = (
                    dresidual_whole
                    - dcoeffs[index] * basis_whole[index]
                    - coeffs[index] * tangents_whole[index]
                )
            newvec_whole = residual_whole / height
            basis_whole.append(newvec_whole)
            tangents_whole.append((dresidual_whole - newvec_whole * dheight) / height)
            hess = hess.at[level + 1, level].set(height)
            dhess = dhess.at[level + 1, level].set(dheight)
    coeff, dcoeff = taylor(hess, dhess)
    spread = jnp.zeros_like(primal)
    dspread = jnp.zeros_like(primal)
    for index in range(KRYLOV):
        spread = spread + coeff[index] * basis[index]
        dspread = dspread + coeff[index] * tangents[index] + dcoeff[index] * basis[index]
    evolved = norm_site * spread
    evolved_tangent = norm_tangent * spread + norm_site * dspread
    return (evolved, evolved_tangent)


def solution(mesh):
    in_specs = (
        P("row", None, "col"),
        P("row", None, "col"),
        P("row", "col"),
        P("row", "col"),
        P(),
        P(),
    )
    out_specs = (P("row", None, "col"), P("row", None, "col"))
    return jax.shard_map(local, mesh=mesh, in_specs=in_specs, out_specs=out_specs, check_vma=False)
```
